768 devices in a mesh: dp: 192 (over y, z, core), mp: 4 (over x).
Axes of the slice: x: 4, y: 8, z: 12, core: 2. Of those that a mesh axis runs over, the one named last changes fastest.
Arguments:
- tokens: bfloat16 [24576, 4096], P('dp'), may hold values from -6 to 6
- blocks: bfloat16 [96, 128, 128], P('mp'), may hold values from -0.5 to 0.5
- block_row: int32 [96], P('mp'), may hold values from -1 to 31, as said below
- block_col: int32 [96], P('mp'), may hold values from -1 to 127, as said below
- cotangent: bfloat16 [24576, 16384], P('dp', 'mp'), may hold values from -6 to 6
Outputs:
- activation: bfloat16 [24576, 16384], P('dp', 'mp')
- input_grad: bfloat16 [24576, 4096], P('dp', 'mp')
- weight_grad: float32 [16, 768, 128], P('mp', 'dp')
The draws below stay inside these ranges and needn't reach their ends.
Inputs may be any that keep to these rules, and one draw needn't show every extreme that they name: `block_row`: slots form 4 x 4 groups of 6: slot (m * 4 + q) * 6 + k. In each group the live slots come first and the others hold -1 in both lists. A live slot of group (m, q) has its column block in q * 32 to q * 32 + 31, and all live slots of one row block lie in groups of one m. No pair of row and column block repeats. For some q all 4 groups (m, q) are full. `block_col`: as for block_row: the two lists are drawn together.
All inputs are finite; a program needn't handle non-finite values.
Results may differ from the reference program's by a relative error of at most 0.0075.
Values may be sent and summed in bfloat16 or wider, within the bound.
No kernel may reach another device: no remote copies, remote signals or barrier semaphores. Data moves between devices by JAX's collectives and lax.ppermute only.
A program may use at most 32 MiB of HBM per device.

```python
import jax
import jax.numpy as jnp
from jax import lax

D = 4096
H = 16384
BS = 128
CAP = 6
NNZ = 96
TOKENS = 24576
N_MP = 4


def layout_lists(key):
    row_count = D // BS
    per_owner = H // BS // N_MP
    folded = jax.random.fold_in(key, 4242)
    key_perm, key_own, key_score, key_live, key_full = jax.random.split(folded, 5)
    order = jax.random.permutation(key_perm, row_count)
    spare_owner = jax.random.randint(key_own, (row_count,), 0, N_MP)
    position = jnp.arange(row_count)
    owner_at = jnp.where(position < 2 * N_MP, position % N_MP, spare_owner).astype(jnp.int32)
    row_owner = jnp.zeros((row_count,), jnp.int32).at[order].set(owner_at)
    pair_count = row_count * per_owner
    pair_index = jnp.arange(pair_count)
    pair_row = pair_index // per_owner
    owner_ids = jnp.arange(N_MP)
    owned_pair = (row_owner[pair_row][None, :] == owner_ids[:, None]).astype(jnp.int32)
    noise_bits = jax.random.randint(key_score, (N_MP, N_MP, pair_count), 0, 1024)
    scores = owned_pair[:, None, :] * 16777216 + noise_bits * 4096 + pair_index[None, None, :]
    chosen = lax.top_k(scores, CAP)[1]
    counts = jax.random.randint(key_live, (N_MP, N_MP), max(CAP // 3, 1), CAP + 1)
    full_owner = jax.random.randint(key_full, (), 0, N_MP)
    counts = jnp.where(owner_ids[None, :] == full_owner, CAP, counts)
    is_alive = jnp.arange(CAP)[None, None, :] < counts[:, :, None]
    row_list = jnp.where(is_alive, chosen // per_owner, -1)
    col_list = jnp.where(is_alive, owner_ids[None, :, None] * per_owner + chosen % per_owner, -1)
    return (row_list.reshape(-1).astype(jnp.int32), col_list.reshape(-1).astype(jnp.int32))


def draw_block_row(key, part):
    return layout_lists(key)[0]


def draw_block_col(key, part):
    return layout_lists(key)[1]


def level_of(key, extent, pieces, least, top_value):
    loudness = 1.0
    for dim, parts in pieces:
        draws = jax.random.uniform(jax.random.fold_in(jax.random.fold_in(key, 6), dim), (parts,), jnp.float32, least / len(pieces), top_value / len(pieces))
        loudness = loudness * jnp.repeat(jnp.exp(draws), extent[dim] // parts).reshape((-1,) + (1,) * (len(extent) - 1 - dim))
    return loudness


def gaussian(own_key, dims, deviation, bound, cuts=(), kind=jnp.bfloat16):
    drawn = jax.random.normal(own_key, dims, jnp.float32) * deviation
    if len(cuts) > 0:
        drawn = level_of(own_key, dims, cuts, -0.22, 0.18) * drawn
    return jnp.clip(drawn, min=-bound, max=bound).astype(kind)


def setup_inputs(seed: int = 0) -> dict:
    streams_of = jax.random.split(jax.random.key(seed), 6)
    return {
        "tokens": gaussian(streams_of[0], (TOKENS, D), 1.0, 6.0, ((0, 192),)),
        "blocks": gaussian(streams_of[1], (NNZ, BS, BS), BS ** -0.5, 0.5, ((0, 4),)),
        "block_row": draw_block_row(jax.random.fold_in(streams_of[5], 71), 0),
        "block_col": draw_block_col(jax.random.fold_in(streams_of[5], 71), 0),
        "cotangent": gaussian(streams_of[4], (TOKENS, H), 1.0, 6.0, ((0, 192), (1, 4))),
    }


def gelu_tanh(inputs):
    return jax.nn.gelu(inputs, approximate=True)

def reference(tokens, blocks, block_row, block_col, cotangent):
    token_count = tokens.shape[0]
    row_count = D // BS
    col_count = H // BS
    spread = tokens.reshape(token_count, row_count, BS)
    live_flag = (block_col >= 0).astype(jnp.float32)
    safe_rows = jnp.maximum(block_row, 0).astype(jnp.int32)
    safe_cols = jnp.maximum(block_col, 0).astype(jnp.int32)

    def forward(carry, payload):
        weight, row_at, col_at, flag = payload
        x_rows = lax.dynamic_index_in_dim(spread, row_at, 1, keepdims=False)
        product = jnp.dot(x_rows, weight, preferred_element_type=jnp.float32)
        product = lax.optimization_barrier(product.astype(jnp.bfloat16)).astype(jnp.float32) * flag
        current = lax.dynamic_index_in_dim(carry, col_at, 1, keepdims=False)
        carry = lax.dynamic_update_index_in_dim(carry, current + product, col_at, 1)
        return (carry, None)
    start = jnp.zeros((token_count, col_count, BS), jnp.float32)
    pre_act, _ = lax.scan(forward, start, (blocks, safe_rows, safe_cols, live_flag))
    pre_flat = pre_act.reshape(token_count, H)
    activation_f, pullback = jax.vjp(gelu_tanh, pre_flat)
    activation = activation_f.astype(jnp.bfloat16)
    pre_grad = pullback(cotangent.astype(jnp.float32))[0].astype(jnp.bfloat16)
    grad_blocks = pre_grad.reshape(token_count, col_count, BS)

    def backward(carry, payload):
        weight, row_at, col_at, flag = payload
        x_rows = lax.dynamic_index_in_dim(spread, row_at, 1, keepdims=False)
        grad_cols = lax.dynamic_index_in_dim(grad_blocks, col_at, 1, keepdims=False)
        term = jnp.dot(grad_cols, weight.T, preferred_element_type=jnp.float32) * flag
        current = lax.dynamic_index_in_dim(carry, row_at, 1, keepdims=False)
        carry = lax.dynamic_update_index_in_dim(carry, current + term, row_at, 1)
        block_grad = jnp.dot(x_rows.T, grad_cols, preferred_element_type=jnp.float32) * flag
        return (carry, block_grad)
    zeros_in = jnp.zeros((token_count, row_count, BS), jnp.float32)
    input_sum, block_grads = lax.scan(backward, zeros_in, (blocks, safe_rows, safe_cols, live_flag))
    input_grad = input_sum.reshape(token_count, D).astype(jnp.bfloat16)
    weight_grad = block_grads.reshape(N_MP * N_MP, CAP * BS, BS)
    return (activation, input_grad, weight_grad)
```

```python
import jax
import jax.numpy as jnp
from jax import lax
from jax.sharding import Mesh, PartitionSpec as P


def gelu_tanh(inputs):
    return jax.nn.gelu(inputs, approximate=True)


def body(tokens, blocks, block_row, block_col, cotangent):
    mp_count = lax.axis_size("mp")
    token_count = tokens.shape[0]
    block_size = blocks.shape[1]
    row_blocks = tokens.shape[1] // block_size
    slot_cap = blocks.shape[0] // mp_count
    col_blocks = cotangent.shape[1] // block_size
    column_here = lax.axis_index("mp")
    spread = tokens.reshape(token_count, row_blocks, block_size)
    w_groups = blocks.reshape(mp_count, slot_cap, block_size, block_size)
    row_groups = jnp.maximum(block_row, 0).reshape(mp_count, slot_cap)
    col_groups = block_col.reshape(mp_count, slot_cap)
    picked_x = jnp.take(spread, row_groups, axis=1)
    live_mask = (col_groups >= 0).astype(jnp.float32)
    own_parts = jnp.einsum(
        "tmck,mckn->mctn", picked_x, w_groups, preferred_element_type=jnp.float32
    )
    own_parts = (own_parts * live_mask[:, :, None, None]).astype(jnp.bfloat16)
    partials, got_cols = (
        lax.all_to_all(own_parts, "mp", split_axis=0, concat_axis=0, tiled=True),
        lax.all_to_all(col_groups, "mp", split_axis=0, concat_axis=0, tiled=True),
    )
    local_col = got_cols - column_here * col_blocks
    onehot = (local_col[:, :, None] == jnp.arange(col_blocks)[None, None, :]).astype(jnp.bfloat16)
    pre_act = jnp.einsum("mctn,mcj->tjn", partials, onehot, preferred_element_type=jnp.float32)
    pre_act = pre_act.reshape(token_count, col_blocks * block_size)
    activation_f, pullback = jax.vjp(gelu_tanh, pre_act)
    activation = activation_f.astype(jnp.bfloat16)
    pre_grad = pullback(cotangent.astype(jnp.float32))[0].astype(jnp.bfloat16)
    pre_grad = pre_grad.reshape(token_count, col_blocks, block_size)
    returned = jnp.einsum(
        "tjn,mcj->mctn", pre_grad, onehot, preferred_element_type=jnp.float32
    ).astype(jnp.bfloat16)
    returned = lax.all_to_all(returned, "mp", split_axis=0, concat_axis=0, tiled=True)
    slot_live = col_groups >= 0
    input_terms = jnp.einsum(
        "mctn,mckn->mctk", returned, w_groups, preferred_element_type=jnp.float32
    )
    row_onehot = (
        (row_groups[:, :, None] == jnp.arange(row_blocks)[None, None, :]) & slot_live[:, :, None]
    ).astype(jnp.float32)
    input_partial = jnp.einsum(
        "mctk,mcr->trk", input_terms, row_onehot, precision=lax.Precision.HIGHEST
    )
    input_partial = input_partial.reshape(token_count, row_blocks * block_size)
    input_grad = lax.psum_scatter(
        input_partial.astype(jnp.bfloat16), "mp", scatter_dimension=1, tiled=True
    )
    weight_terms = jnp.einsum(
        "tmck,mctn->mckn", picked_x, returned, preferred_element_type=jnp.float32
    )
    weight_terms = weight_terms.reshape(mp_count, slot_cap * block_size, block_size)
    ny, nz, nc = lax.axis_size("y"), lax.axis_size("z"), lax.axis_size("c")
    rows = slot_cap * block_size // (ny * nz * nc)
    staged = weight_terms.reshape(mp_count, ny, nz, nc, rows, block_size)
    staged = jnp.transpose(staged, (3, 2, 1, 4, 0, 5)).reshape(-1, mp_count, block_size)
    for axis in ("c", "z", "y"):
        staged = lax.psum_scatter(staged, axis, scatter_dimension=0, tiled=True)
    summed = jnp.transpose(staged, (1, 0, 2))
    return (activation, input_grad, summed)


def solution(mesh):
    dp_count, mp_count = mesh.devices.shape
    y_count = len({d.coords[1] for d in mesh.devices.flat})
    chip_cores = len({d.core_on_chip for d in mesh.devices.flat})
    grid = mesh.devices.reshape(y_count, dp_count // (y_count * chip_cores), chip_cores, mp_count)
    split = Mesh(grid, ("y", "z", "c", "mp"))
    dp = ("y", "z", "c")
    placed = (P(dp, None), P("mp", None, None), P("mp"), P("mp"), P(dp, "mp"))
    return jax.shard_map(
        body,
        mesh=split,
        in_specs=placed,
        out_specs=(P(dp, "mp"), P(dp, "mp"), P("mp", dp, None)),
        check_vma=False,
    )
```

```python
import jax
import jax.numpy as jnp
from jax import lax
from jax.sharding import Mesh, PartitionSpec as P


def gelu_tanh(inputs):
    return jax.nn.gelu(inputs, approximate=True)


def body(tokens, blocks, block_row, block_col, cotangent):
    mp_count = lax.axis_size("mp")
    token_count = tokens.shape[0]
    block_size = blocks.shape[1]
    row_blocks = tokens.shape[1] // block_size
    slot_cap = blocks.shape[0] // mp_count
    col_blocks = cotangent.shape[1] // block_size
    column_here = lax.axis_index("mp")
    spread = tokens.reshape(token_count, row_blocks, block_size)
    w_groups = blocks.reshape(mp_count, slot_cap, block_size, block_size)
    row_groups = jnp.maximum(block_row, 0).reshape(mp_count, slot_cap)
    col_groups = block_col.reshape(mp_count, slot_cap)
    picked_x = jnp.take(spread, row_groups, axis=1)
    live_mask = (col_groups >= 0).astype(jnp.float32)
    own_parts = jnp.einsum(
        "tmck,mckn->mctn", picked_x, w_groups, preferred_element_type=jnp.float32
    )
    own_parts = (own_parts * live_mask[:, :, None, None]).astype(jnp.bfloat16)
    partials, got_cols = (
        lax.all_to_all(own_parts, "mp", split_axis=0, concat_axis=0, tiled=True),
        lax.all_to_all(col_groups, "mp", split_axis=0, concat_axis=0, tiled=True),
    )
    local_col = got_cols - column_here * col_blocks
    onehot = (local_col[:, :, None] == jnp.arange(col_blocks)[None, None, :]).astype(jnp.bfloat16)
    pre_act = jnp.einsum("mctn,mcj->tjn", partials, onehot, preferred_element_type=jnp.float32)
    pre_act = pre_act.reshape(token_count, col_blocks * block_size)
    activation_f, pullback = jax.vjp(gelu_tanh, pre_act)
    activation = activation_f.astype(jnp.bfloat16)
    pre_grad = pullback(cotangent.astype(jnp.float32))[0].astype(jnp.bfloat16)
    pre_grad = pre_grad.reshape(token_count, col_blocks, block_size)
    returned = jnp.einsum(
        "tjn,mcj->mctn", pre_grad, onehot, preferred_element_type=jnp.float32
    ).astype(jnp.bfloat16)
    returned = lax.all_to_all(returned, "mp", split_axis=0, concat_axis=0, tiled=True)
    slot_live = col_groups >= 0
    input_terms = jnp.einsum(
        "mctn,mckn->mctk", returned, w_groups, preferred_element_type=jnp.float32
    )
    row_onehot = (
        (row_groups[:, :, None] == jnp.arange(row_blocks)[None, None, :]) & slot_live[:, :, None]
    ).astype(jnp.float32)
    input_partial = jnp.einsum(
        "mctk,mcr->trk", input_terms, row_onehot, precision=lax.Precision.HIGHEST
    )
    input_partial = input_partial.reshape(token_count, row_blocks * block_size)
    input_grad = lax.psum_scatter(
        input_partial.astype(jnp.bfloat16), "mp", scatter_dimension=1, tiled=True
    )
    weight_terms = jnp.einsum(
        "tmck,mctn->mckn", picked_x, returned, preferred_element_type=jnp.float32
    )
    weight_terms = weight_terms.reshape(mp_count, slot_cap * block_size, block_size)
    ny, nz, nc = lax.axis_size("y"), lax.axis_size("z"), lax.axis_size("c")
    rows = slot_cap * block_size // (ny * nz * nc)
    staged = weight_terms.reshape(mp_count, ny, nz, nc, rows, block_size)
    staged = jnp.transpose(staged, (3, 1, 2, 4, 0, 5)).reshape(nc, -1, mp_count, block_size)
    staged = lax.all_to_all(staged, "c", 0, 0, tiled=True).sum(0)
    staged = staged.reshape(ny * nz, rows, mp_count, block_size)
    staged = lax.all_to_all(staged, ("y", "z"), 0, 0, tiled=True).sum(0)
    summed = jnp.transpose(staged, (1, 0, 2))
    return (activation, input_grad, summed)


def solution(mesh):
    dp_count, mp_count = mesh.devices.shape
    y_count = len({d.coords[1] for d in mesh.devices.flat})
    chip_cores = len({d.core_on_chip for d in mesh.devices.flat})
    grid = mesh.devices.reshape(y_count, dp_count // (y_count * chip_cores), chip_cores, mp_count)
    split = Mesh(grid, ("y", "z", "c", "mp"))
    dp = ("y", "z", "c")
    placed = (P(dp, None), P("mp", None, None), P("mp"), P("mp"), P(dp, "mp"))
    return jax.shard_map(
        body,
        mesh=split,
        in_specs=placed,
        out_specs=(P(dp, "mp"), P(dp, "mp"), P("mp", dp, None)),
        check_vma=False,
    )
```

```python
import jax
import jax.numpy as jnp
from jax import lax
from jax.sharding import Mesh, PartitionSpec as P


def gelu_tanh(inputs):
    return jax.nn.gelu(inputs, approximate=True)


def body(tokens, blocks, block_row, block_col, cotangent):
    mp_count = lax.axis_size("mp")
    token_count = tokens.shape[0]
    block_size = blocks.shape[1]
    row_blocks = tokens.shape[1] // block_size
    slot_cap = blocks.shape[0] // mp_count
    col_blocks = cotangent.shape[1] // block_size
    column_here = lax.axis_index("mp")
    w_groups = blocks.reshape(mp_count, slot_cap, block_size, block_size)
    w_here = lax.all_to_all(w_groups, "mp", 0, 0, tiled=True)
    lists = jnp.stack([block_row, block_col]).reshape(2, mp_count, slot_cap)
    lists = lax.all_to_all(lists, "mp", 1, 1, tiled=True)
    row_groups = jnp.maximum(lists[0], 0)
    col_groups = lists[1]
    slot_live = col_groups >= 0
    spread = tokens.reshape(token_count, row_blocks, block_size)
    picked_x = jnp.take(spread, row_groups, axis=1)
    live_mask = slot_live.astype(jnp.float32)
    parts = jnp.einsum(
        "tmck,mckn->mctn", picked_x, w_here, preferred_element_type=jnp.float32
    )
    parts = (parts * live_mask[:, :, None, None]).astype(jnp.bfloat16)
    local_col = col_groups - column_here * col_blocks
    onehot = (local_col[:, :, None] == jnp.arange(col_blocks)[None, None, :]).astype(jnp.bfloat16)
    pre_act = jnp.einsum("mctn,mcj->tjn", parts, onehot, preferred_element_type=jnp.float32)
    pre_act = pre_act.reshape(token_count, col_blocks * block_size)
    activation_f, pullback = jax.vjp(gelu_tanh, pre_act)
    activation = activation_f.astype(jnp.bfloat16)
    pre_grad = pullback(cotangent.astype(jnp.float32))[0].astype(jnp.bfloat16)
    pre_grad = pre_grad.reshape(token_count, col_blocks, block_size)
    grad_cols = jnp.einsum(
        "tjn,mcj->mctn", pre_grad, onehot, preferred_element_type=jnp.float32
    ).astype(jnp.bfloat16)
    input_terms = jnp.einsum(
        "mctn,mckn->mctk", grad_cols, w_here, preferred_element_type=jnp.float32
    )
    row_onehot = (
        (row_groups[:, :, None] == jnp.arange(row_blocks)[None, None, :]) & slot_live[:, :, None]
    ).astype(jnp.float32)
    input_partial = jnp.einsum(
        "mctk,mcr->trk", input_terms, row_onehot, precision=lax.Precision.HIGHEST
    )
    input_partial = input_partial.reshape(token_count, mp_count, row_blocks * block_size // mp_count)
    input_partial = lax.all_to_all(input_partial, "mp", 1, 1, tiled=True)
    input_grad = input_partial.sum(1).astype(jnp.bfloat16)
    weight_terms = jnp.einsum(
        "tmck,mctn->mckn", picked_x, grad_cols, preferred_element_type=jnp.float32
    )
    weight_terms = weight_terms.reshape(mp_count, slot_cap * block_size, block_size)
    ny, nz, nc = lax.axis_size("y"), lax.axis_size("z"), lax.axis_size("c")
    rows = slot_cap * block_size // (ny * nz * nc)
    staged = weight_terms.reshape(mp_count, ny, nz, nc, rows, block_size)
    staged = jnp.transpose(staged, (3, 1, 2, 4, 0, 5)).reshape(nc, -1, mp_count, block_size)
    staged = lax.all_to_all(staged, "c", 0, 0, tiled=True).sum(0)
    staged = staged.reshape(ny * nz, rows, mp_count, block_size)
    staged = lax.all_to_all(staged, ("y", "z"), 0, 0, tiled=True).sum(0)
    staged = lax.all_to_all(staged, "mp", 1, 1, tiled=True)
    summed = jnp.transpose(staged, (1, 0, 2))
    return (activation, input_grad, summed)


def solution(mesh):
    dp_count, mp_count = mesh.devices.shape
    y_count = len({d.coords[1] for d in mesh.devices.flat})
    chip_cores = len({d.core_on_chip for d in mesh.devices.flat})
    grid = mesh.devices.reshape(y_count, dp_count // (y_count * chip_cores), chip_cores, mp_count)
    split = Mesh(grid, ("y", "z", "c", "mp"))
    dp = ("y", "z", "c")
    placed = (P(dp, None), P("mp", None, None), P("mp"), P("mp"), P(dp, "mp"))
    return jax.shard_map(
        body,
        mesh=split,
        in_specs=placed,
        out_specs=(P(dp, "mp"), P(dp, "mp"), P("mp", dp, None)),
        check_vma=False,
    )
```

```python
import jax
import jax.numpy as jnp
from jax import lax
from jax.sharding import Mesh, PartitionSpec as P


def gelu_tanh(inputs):
    return jax.nn.gelu(inputs, approximate=True)


def body(tokens, blocks, block_row, block_col, cotangent):
    mp_count = lax.axis_size("mp")
    token_count = tokens.shape[0]
    block_size = blocks.shape[1]
    row_blocks = tokens.shape[1] // block_size
    slot_cap = blocks.shape[0] // mp_count
    col_blocks = cotangent.shape[1] // block_size
    column_here = lax.axis_index("mp")
    w_groups = blocks.reshape(mp_count, slot_cap * block_size, block_size)
    lists = jnp.stack([block_row, block_col], 1).reshape(mp_count, 1, slot_cap * 2)
    lists = jnp.pad(lists.astype(jnp.bfloat16), ((0, 0), (0, 15), (0, block_size - slot_cap * 2)))
    sent = lax.all_to_all(jnp.concatenate([w_groups, lists], 1), "mp", 0, 0, tiled=True)
    w_here = sent[:, : slot_cap * block_size].reshape(mp_count, slot_cap, block_size, block_size)
    lists = sent[:, slot_cap * block_size, : slot_cap * 2].astype(jnp.int32).reshape(mp_count, slot_cap, 2)
    row_groups = jnp.maximum(lists[:, :, 0], 0)
    col_groups = lists[:, :, 1]
    slot_live = col_groups >= 0
    spread = tokens.reshape(token_count, row_blocks, block_size)
    picked_x = jnp.take(spread, row_groups, axis=1)
    live_mask = slot_live.astype(jnp.float32)
    parts = jnp.einsum(
        "tmck,mckn->mctn", picked_x, w_here, preferred_element_type=jnp.float32
    )
    parts = (parts * live_mask[:, :, None, None]).astype(jnp.bfloat16)
    local_col = col_groups - column_here * col_blocks
    onehot = (local_col[:, :, None] == jnp.arange(col_blocks)[None, None, :]).astype(jnp.bfloat16)
    pre_act = jnp.einsum("mctn,mcj->tjn", parts, onehot, preferred_element_type=jnp.float32)
    pre_act = pre_act.reshape(token_count, col_blocks * block_size)
    activation_f, pullback = jax.vjp(gelu_tanh, pre_act)
    activation = activation_f.astype(jnp.bfloat16)
    pre_grad = pullback(cotangent.astype(jnp.float32))[0].astype(jnp.bfloat16)
    pre_grad = pre_grad.reshape(token_count, col_blocks, block_size)
    grad_cols = jnp.einsum(
        "tjn,mcj->mctn", pre_grad, onehot, preferred_element_type=jnp.float32
    ).astype(jnp.bfloat16)
    input_terms = jnp.einsum(
        "mctn,mckn->mctk", grad_cols, w_here, preferred_element_type=jnp.float32
    )
    row_onehot = (
        (row_groups[:, :, None] == jnp.arange(row_blocks)[None, None, :]) & slot_live[:, :, None]
    ).astype(jnp.float32)
    input_partial = jnp.einsum(
        "mctk,mcr->trk", input_terms, row_onehot, precision=lax.Precision.HIGHEST
    )
    input_partial = input_partial.reshape(token_count, row_blocks * block_size)
    input_grad = lax.psum_scatter(input_partial, "mp", scatter_dimension=1, tiled=True)
    input_grad = input_grad.astype(jnp.bfloat16)
    weight_terms = jnp.einsum(
        "tmck,mctn->mckn", picked_x, grad_cols, preferred_element_type=jnp.float32
    )
    weight_terms = weight_terms.reshape(mp_count, slot_cap * block_size, block_size)
    ny, nz, nc = lax.axis_size("y"), lax.axis_size("z"), lax.axis_size("c")
    rows = slot_cap * block_size // (ny * nz * nc)
    staged = weight_terms.reshape(mp_count, ny, nz, nc, rows, block_size)
    staged = jnp.transpose(staged, (3, 1, 2, 4, 0, 5)).reshape(nc, -1, mp_count, block_size)
    staged = lax.all_to_all(staged, "c", 0, 0, tiled=True).sum(0)
    staged = staged.reshape(ny * nz, rows, mp_count, block_size)
    staged = lax.all_to_all(staged, ("y", "z"), 0, 0, tiled=True).sum(0)
    staged = lax.all_to_all(staged, "mp", 1, 1, tiled=True)
    summed = jnp.transpose(staged, (1, 0, 2))
    return (activation, input_grad, summed)


def solution(mesh):
    dp_count, mp_count = mesh.devices.shape
    y_count = len({d.coords[1] for d in mesh.devices.flat})
    chip_cores = len({d.core_on_chip for d in mesh.devices.flat})
    grid = mesh.devices.reshape(y_count, dp_count // (y_count * chip_cores), chip_cores, mp_count)
    split = Mesh(grid, ("y", "z", "c", "mp"))
    dp = ("y", "z", "c")
    placed = (P(dp, None), P("mp", None, None), P("mp"), P("mp"), P(dp, "mp"))
    return jax.shard_map(
        body,
        mesh=split,
        in_specs=placed,
        out_specs=(P(dp, "mp"), P(dp, "mp"), P("mp", dp, None)),
        check_vma=False,
    )
```

```python
import jax
import jax.numpy as jnp
from jax import lax
from jax.sharding import Mesh, PartitionSpec as P


def gelu_tanh(inputs):
    return jax.nn.gelu(inputs, approximate=True)


def body(tokens, blocks, block_row, block_col, cotangent):
    mp_count = lax.axis_size("mp")
    token_count = tokens.shape[0]
    block_size = blocks.shape[1]
    row_blocks = tokens.shape[1] // block_size
    slot_cap = blocks.shape[0] // mp_count
    col_blocks = cotangent.shape[1] // block_size
    column_here = lax.axis_index("mp")
    w_groups = blocks.reshape(mp_count, slot_cap * block_size, block_size)
    lists = jnp.stack([block_row, block_col], 1).reshape(mp_count, 1, slot_cap * 2)
    lists = jnp.pad(lists.astype(jnp.bfloat16), ((0, 0), (0, 15), (0, block_size - slot_cap * 2)))
    sent = lax.all_to_all(jnp.concatenate([w_groups, lists], 1), "mp", 0, 0, tiled=True)
    w_here = sent[:, : slot_cap * block_size].reshape(mp_count, slot_cap, block_size, block_size)
    lists = sent[:, slot_cap * block_size, : slot_cap * 2].astype(jnp.int32).reshape(mp_count, slot_cap, 2)
    row_groups = jnp.maximum(lists[:, :, 0], 0)
    col_groups = lists[:, :, 1]
    slot_live = col_groups >= 0
    spread = tokens.reshape(token_count, row_blocks, block_size)
    picked_x = jnp.take(spread, row_groups, axis=1)
    live_mask = slot_live.astype(jnp.float32)
    parts = jnp.einsum(
        "tmck,mckn->mctn", picked_x, w_here, preferred_element_type=jnp.float32
    )
    parts = (parts * live_mask[:, :, None, None]).astype(jnp.bfloat16)
    local_col = col_groups - column_here * col_blocks
    onehot = (local_col[:, :, None] == jnp.arange(col_blocks)[None, None, :]).astype(jnp.bfloat16)
    pre_act = jnp.einsum("mctn,mcj->tjn", parts, onehot, preferred_element_type=jnp.float32)
    pre_act = pre_act.reshape(token_count, col_blocks * block_size)
    activation_f, pullback = jax.vjp(gelu_tanh, pre_act)
    activation = activation_f.astype(jnp.bfloat16)
    pre_grad = pullback(cotangent.astype(jnp.float32))[0].astype(jnp.bfloat16)
    pre_grad = pre_grad.reshape(token_count, col_blocks, block_size)
    grad_cols = jnp.einsum(
        "tjn,mcj->mctn", pre_grad, onehot, preferred_element_type=jnp.float32
    ).astype(jnp.bfloat16)
    input_terms = jnp.einsum(
        "mctn,mckn->mctk", grad_cols, w_here, preferred_element_type=jnp.float32
    )
    row_onehot = (
        (row_groups[:, :, None] == jnp.arange(row_blocks)[None, None, :]) & slot_live[:, :, None]
    ).astype(jnp.float32)
    input_partial = jnp.einsum(
        "mctk,mcr->trk", input_terms, row_onehot, precision=lax.Precision.HIGHEST
    )
    input_partial = input_partial.reshape(token_count, row_blocks * block_size)
    input_grad = lax.psum_scatter(input_partial, "mp", scatter_dimension=1, tiled=True)
    input_grad = input_grad.astype(jnp.bfloat16)
    weight_terms = jnp.einsum(
        "tmck,mctn->mckn", picked_x, grad_cols, preferred_element_type=jnp.float32
    )
    weight_terms = weight_terms.reshape(mp_count, slot_cap * block_size, block_size)
    ny, nz, nc = lax.axis_size("y"), lax.axis_size("z"), lax.axis_size("c")
    rows = slot_cap * block_size // (ny * nz * nc)
    staged = weight_terms.reshape(mp_count, ny, nz, nc, rows, block_size)
    staged = jnp.transpose(staged, (3, 1, 2, 4, 0, 5)).reshape(nc, -1, mp_count, block_size)
    staged = lax.all_to_all(staged, "c", 0, 0, tiled=True).sum(0)
    staged = staged.reshape(ny * nz, rows, mp_count, block_size)
    staged = lax.all_to_all(staged.astype(jnp.bfloat16), ("y", "z"), 0, 0, tiled=True)
    staged = staged.astype(jnp.float32).sum(0)
    staged = lax.all_to_all(staged, "mp", 1, 1, tiled=True)
    summed = jnp.transpose(staged, (1, 0, 2))
    return (activation, input_grad, summed)


def solution(mesh):
    dp_count, mp_count = mesh.devices.shape
    y_count = len({d.coords[1] for d in mesh.devices.flat})
    chip_cores = len({d.core_on_chip for d in mesh.devices.flat})
    grid = mesh.devices.reshape(y_count, dp_count // (y_count * chip_cores), chip_cores, mp_count)
    split = Mesh(grid, ("y", "z", "c", "mp"))
    dp = ("y", "z", "c")
    placed = (P(dp, None), P("mp", None, None), P("mp"), P("mp"), P(dp, "mp"))
    return jax.shard_map(
        body,
        mesh=split,
        in_specs=placed,
        out_specs=(P(dp, "mp"), P(dp, "mp"), P("mp", dp, None)),
        check_vma=False,
    )
```

```python
import jax
import jax.numpy as jnp
from jax import lax
from jax.sharding import Mesh, PartitionSpec as P


def gelu_tanh(inputs):
    return jax.nn.gelu(inputs, approximate=True)


def body(tokens, blocks, block_row, block_col, cotangent):
    mp_count = lax.axis_size("mp")
    token_count = tokens.shape[0]
    block_size = blocks.shape[1]
    row_blocks = tokens.shape[1] // block_size
    slot_cap = blocks.shape[0] // mp_count
    col_blocks = cotangent.shape[1] // block_size
    column_here = lax.axis_index("mp")
    w_groups = blocks.reshape(mp_count, slot_cap * block_size, block_size)
    lists = jnp.stack([block_row, block_col], 1).reshape(mp_count, 1, slot_cap * 2)
    lists = jnp.pad(lists.astype(jnp.bfloat16), ((0, 0), (0, 15), (0, block_size - slot_cap * 2)))
    sent = lax.all_to_all(jnp.concatenate([w_groups, lists], 1), "mp", 0, 0, tiled=True)
    w_here = sent[:, : slot_cap * block_size].reshape(mp_count, slot_cap, block_size, block_size)
    lists = sent[:, slot_cap * block_size, : slot_cap * 2].astype(jnp.int32).reshape(mp_count, slot_cap, 2)
    row_groups = jnp.maximum(lists[:, :, 0], 0)
    col_groups = lists[:, :, 1]
    slot_live = col_groups >= 0
    spread = tokens.reshape(token_count, row_blocks, block_size)
    picked_x = jnp.take(spread, row_groups, axis=1)
    live_mask = slot_live.astype(jnp.float32)
    parts = jnp.einsum(
        "tmck,mckn->mctn", picked_x, w_here, preferred_element_type=jnp.float32
    )
    parts = (parts * live_mask[:, :, None, None]).astype(jnp.bfloat16)
    local_col = col_groups - column_here * col_blocks
    onehot = (local_col[:, :, None] == jnp.arange(col_blocks)[None, None, :]).astype(jnp.bfloat16)
    pre_act = jnp.einsum("mctn,mcj->tjn", parts, onehot, preferred_element_type=jnp.float32)
    pre_act = pre_act.reshape(token_count, col_blocks * block_size)
    activation_f, pullback = jax.vjp(gelu_tanh, pre_act)
    activation = activation_f.astype(jnp.bfloat16)
    pre_grad = pullback(cotangent.astype(jnp.float32))[0].astype(jnp.bfloat16)
    pre_grad = pre_grad.reshape(token_count, col_blocks, block_size)
    grad_cols = jnp.einsum(
        "tjn,mcj->mctn", pre_grad, onehot, preferred_element_type=jnp.float32
    ).astype(jnp.bfloat16)
    input_terms = jnp.einsum(
        "mctn,mckn->mctk", grad_cols, w_here, preferred_element_type=jnp.float32
    )
    row_onehot = (
        (row_groups[:, :, None] == jnp.arange(row_blocks)[None, None, :]) & slot_live[:, :, None]
    ).astype(jnp.float32)
    input_partial = jnp.einsum(
        "mctk,mcr->rtk", input_terms, row_onehot, precision=lax.Precision.HIGHEST
    )
    input_grad = lax.psum_scatter(input_partial, "mp", scatter_dimension=0, tiled=True)
    input_grad = jnp.transpose(input_grad.astype(jnp.bfloat16), (1, 0, 2))
    input_grad = input_grad.reshape(token_count, row_blocks * block_size // mp_count)
    weight_terms = jnp.einsum(
        "tmck,mctn->mckn", picked_x, grad_cols, preferred_element_type=jnp.float32
    )
    weight_terms = weight_terms.reshape(mp_count, slot_cap * block_size, block_size)
    ny, nz, nc = lax.axis_size("y"), lax.axis_size("z"), lax.axis_size("c")
    rows = slot_cap * block_size // (ny * nz * nc)
    staged = weight_terms.reshape(mp_count, ny, nz, nc, rows, block_size)
    staged = jnp.transpose(staged, (3, 1, 2, 4, 0, 5)).reshape(nc, -1, mp_count, block_size)
    staged = lax.all_to_all(staged, "c", 0, 0, tiled=True).sum(0)
    staged = staged.reshape(ny * nz, rows, mp_count, block_size)
    staged = lax.all_to_all(staged.astype(jnp.bfloat16), ("y", "z"), 0, 0, tiled=True)
    staged = staged.astype(jnp.float32).sum(0)
    staged = lax.all_to_all(staged, "mp", 1, 1, tiled=True)
    summed = jnp.transpose(staged, (1, 0, 2))
    return (activation, input_grad, summed)


def solution(mesh):
    dp_count, mp_count = mesh.devices.shape
    y_count = len({d.coords[1] for d in mesh.devices.flat})
    chip_cores = len({d.core_on_chip for d in mesh.devices.flat})
    grid = mesh.devices.reshape(y_count, dp_count // (y_count * chip_cores), chip_cores, mp_count)
    split = Mesh(grid, ("y", "z", "c", "mp"))
    dp = ("y", "z", "c")
    placed = (P(dp, None), P("mp", None, None), P("mp"), P("mp"), P(dp, "mp"))
    return jax.shard_map(
        body,
        mesh=split,
        in_specs=placed,
        out_specs=(P(dp, "mp"), P(dp, "mp"), P("mp", dp, None)),
        check_vma=False,
    )
```

```python
import jax
import jax.numpy as jnp
from jax import lax
from jax.sharding import Mesh, PartitionSpec as P


def gelu_tanh(inputs):
    return jax.nn.gelu(inputs, approximate=True)


def body(tokens, blocks, block_row, block_col, cotangent):
    mp_count = lax.axis_size("mp")
    token_count = tokens.shape[0]
    block_size = blocks.shape[1]
    row_blocks = tokens.shape[1] // block_size
    slot_cap = blocks.shape[0] // mp_count
    col_blocks = cotangent.shape[1] // block_size
    column_here = lax.axis_index("mp")
    w_groups = blocks.reshape(mp_count, slot_cap * block_size, block_size)
    lists = jnp.stack([block_row, block_col], 1).reshape(mp_count, 1, slot_cap * 2)
    lists = jnp.pad(lists.astype(jnp.bfloat16), ((0, 0), (0, 15), (0, block_size - slot_cap * 2)))
    sent = lax.all_to_all(jnp.concatenate([w_groups, lists], 1), "mp", 0, 0, tiled=True)
    w_here = sent[:, : slot_cap * block_size].reshape(mp_count, slot_cap, block_size, block_size)
    lists = sent[:, slot_cap * block_size, : slot_cap * 2].astype(jnp.int32).reshape(mp_count, slot_cap, 2)
    row_groups = jnp.maximum(lists[:, :, 0], 0)
    col_groups = lists[:, :, 1]
    slot_live = col_groups >= 0
    spread = tokens.reshape(token_count, row_blocks, block_size)
    picked_x = jnp.take(spread, row_groups, axis=1)
    live_mask = slot_live.astype(jnp.float32)
    parts = jnp.einsum(
        "tmck,mckn->mctn", picked_x, w_here, preferred_element_type=jnp.float32
    )
    parts = (parts * live_mask[:, :, None, None]).astype(jnp.bfloat16)
    local_col = col_groups - column_here * col_blocks
    onehot = (local_col[:, :, None] == jnp.arange(col_blocks)[None, None, :]).astype(jnp.bfloat16)
    pre_act = jnp.einsum("mctn,mcj->tjn", parts, onehot, preferred_element_type=jnp.float32)
    pre_act = pre_act.reshape(token_count, col_blocks * block_size)
    activation_f, pullback = jax.vjp(gelu_tanh, pre_act)
    activation = activation_f.astype(jnp.bfloat16)
    pre_grad = pullback(cotangent.astype(jnp.float32))[0].astype(jnp.bfloat16)
    pre_grad = pre_grad.reshape(token_count, col_blocks, block_size)
    grad_cols = jnp.einsum(
        "tjn,mcj->mctn", pre_grad, onehot, preferred_element_type=jnp.float32
    ).astype(jnp.bfloat16)
    input_terms = jnp.einsum(
        "mctn,mckn->mctk", grad_cols, w_here, preferred_element_type=jnp.float32
    )
    row_onehot = (
        (row_groups[:, :, None] == jnp.arange(row_blocks)[None, None, :]) & slot_live[:, :, None]
    ).astype(jnp.float32)
    input_partial = jnp.einsum(
        "mctk,mcr->rtk", input_terms, row_onehot, precision=lax.Precision.HIGHEST
    )
    pieces = input_partial.reshape(mp_count, row_blocks // mp_count, token_count, block_size)
    input_grad = lax.dynamic_index_in_dim(pieces, column_here, 0, keepdims=False)
    for shift in range(1, mp_count):
        piece = lax.dynamic_index_in_dim(pieces, (column_here + shift) % mp_count, 0, keepdims=False)
        ring = [(k, (k + shift) % mp_count) for k in range(mp_count)]
        input_grad = input_grad + lax.ppermute(piece, "mp", ring)
    input_grad = jnp.transpose(input_grad.astype(jnp.bfloat16), (1, 0, 2))
    input_grad = input_grad.reshape(token_count, row_blocks * block_size // mp_count)
    weight_terms = jnp.einsum(
        "tmck,mctn->mckn", picked_x, grad_cols, preferred_element_type=jnp.float32
    )
    weight_terms = weight_terms.reshape(mp_count, slot_cap * block_size, block_size)
    ny, nz, nc = lax.axis_size("y"), lax.axis_size("z"), lax.axis_size("c")
    rows = slot_cap * block_size // (ny * nz * nc)
    staged = weight_terms.reshape(mp_count, ny, nz, nc, rows, block_size)
    staged = jnp.transpose(staged, (3, 1, 2, 4, 0, 5)).reshape(nc, -1, mp_count, block_size)
    staged = lax.all_to_all(staged, "c", 0, 0, tiled=True).sum(0)
    staged = staged.reshape(ny * nz, rows, mp_count, block_size)
    staged = lax.all_to_all(staged.astype(jnp.bfloat16), ("y", "z"), 0, 0, tiled=True)
    staged = staged.astype(jnp.float32).sum(0)
    staged = lax.all_to_all(staged, "mp", 1, 1, tiled=True)
    summed = jnp.transpose(staged, (1, 0, 2))
    return (activation, input_grad, summed)


def solution(mesh):
    dp_count, mp_count = mesh.devices.shape
    y_count = len({d.coords[1] for d in mesh.devices.flat})
    chip_cores = len({d.core_on_chip for d in mesh.devices.flat})
    grid = mesh.devices.reshape(y_count, dp_count // (y_count * chip_cores), chip_cores, mp_count)
    split = Mesh(grid, ("y", "z", "c", "mp"))
    dp = ("y", "z", "c")
    placed = (P(dp, None), P("mp", None, None), P("mp"), P("mp"), P(dp, "mp"))
    return jax.shard_map(
        body,
        mesh=split,
        in_specs=placed,
        out_specs=(P(dp, "mp"), P(dp, "mp"), P("mp", dp, None)),
        check_vma=False,
    )
```

```python
import jax
import jax.numpy as jnp
from jax import lax
from jax.sharding import Mesh, PartitionSpec as P


def gelu_tanh(inputs):
    return jax.nn.gelu(inputs, approximate=True)


def body(tokens, blocks, block_row, block_col, cotangent):
    mp_count = lax.axis_size("mp")
    token_count = tokens.shape[0]
    block_size = blocks.shape[1]
    row_blocks = tokens.shape[1] // block_size
    slot_cap = blocks.shape[0] // mp_count
    col_blocks = cotangent.shape[1] // block_size
    column_here = lax.axis_index("mp")
    w_groups = blocks.reshape(mp_count, slot_cap * block_size, block_size)
    lists = jnp.stack([block_row, block_col], 1).reshape(mp_count, 1, slot_cap * 2)
    lists = jnp.pad(lists.astype(jnp.bfloat16), ((0, 0), (0, 15), (0, block_size - slot_cap * 2)))
    sent = lax.all_to_all(jnp.concatenate([w_groups, lists], 1), "mp", 0, 0, tiled=True)
    w_here = sent[:, : slot_cap * block_size].reshape(mp_count, slot_cap, block_size, block_size)
    lists = sent[:, slot_cap * block_size, : slot_cap * 2].astype(jnp.int32).reshape(mp_count, slot_cap, 2)
    row_groups = jnp.maximum(lists[:, :, 0], 0)
    col_groups = lists[:, :, 1]
    slot_live = col_groups >= 0
    spread = tokens.reshape(token_count, row_blocks, block_size)
    picked_x = jnp.take(spread, row_groups, axis=1)
    live_mask = slot_live.astype(jnp.float32)
    parts = jnp.einsum(
        "tmck,mckn->mctn", picked_x, w_here, preferred_element_type=jnp.float32
    )
    parts = (parts * live_mask[:, :, None, None]).astype(jnp.bfloat16)
    local_col = col_groups - column_here * col_blocks
    onehot = (local_col[:, :, None] == jnp.arange(col_blocks)[None, None, :]).astype(jnp.bfloat16)
    pre_act = jnp.einsum("mctn,mcj->tjn", parts, onehot, preferred_element_type=jnp.float32)
    pre_act = pre_act.reshape(token_count, col_blocks * block_size)
    activation_f, pullback = jax.vjp(gelu_tanh, pre_act)
    activation = activation_f.astype(jnp.bfloat16)
    pre_grad = pullback(cotangent.astype(jnp.float32))[0].astype(jnp.bfloat16)
    pre_grad = pre_grad.reshape(token_count, col_blocks, block_size)
    grad_cols = jnp.einsum(
        "tjn,mcj->mctn", pre_grad, onehot, preferred_element_type=jnp.float32
    ).astype(jnp.bfloat16)
    input_terms = jnp.einsum(
        "mctn,mckn->mctk", grad_cols, w_here, preferred_element_type=jnp.float32
    )
    local_row = (row_groups - column_here * (row_blocks // mp_count)) % row_blocks
    row_onehot = (
        (local_row[:, :, None] == jnp.arange(row_blocks)[None, None, :]) & slot_live[:, :, None]
    ).astype(jnp.float32)
    input_partial = jnp.einsum(
        "mctk,mcr->rtk", input_terms, row_onehot, precision=lax.Precision.HIGHEST
    )
    pieces = input_partial.reshape(mp_count, row_blocks // mp_count, token_count, block_size)
    weight_terms = jnp.einsum(
        "tmck,mctn->mckn", picked_x, grad_cols, preferred_element_type=jnp.float32
    )
    weight_terms = weight_terms.reshape(mp_count, slot_cap * block_size, block_size)
    weight_terms, pieces = lax.optimization_barrier((weight_terms, pieces))
    input_grad = pieces[0]
    for shift in range(1, mp_count):
        ring = [(k, (k + shift) % mp_count) for k in range(mp_count)]
        input_grad = input_grad + lax.ppermute(pieces[shift], "mp", ring)
    input_grad = jnp.transpose(input_grad.astype(jnp.bfloat16), (1, 0, 2))
    input_grad = input_grad.reshape(token_count, row_blocks * block_size // mp_count)
    ny, nz, nc = lax.axis_size("y"), lax.axis_size("z"), lax.axis_size("c")
    rows = slot_cap * block_size // (ny * nz * nc)
    staged = weight_terms.reshape(mp_count, ny, nz, nc, rows, block_size)
    staged = jnp.transpose(staged, (3, 1, 2, 4, 0, 5)).reshape(nc, -1, mp_count, block_size)
    staged = lax.all_to_all(staged, "c", 0, 0, tiled=True).sum(0)
    staged = staged.reshape(ny * nz, rows, mp_count, block_size)
    staged = lax.all_to_all(staged.astype(jnp.bfloat16), ("y", "z"), 0, 0, tiled=True)
    staged = staged.astype(jnp.float32).sum(0)
    staged = lax.all_to_all(staged, "mp", 1, 1, tiled=True)
    summed = jnp.transpose(staged, (1, 0, 2))
    return (activation, input_grad, summed)


def solution(mesh):
    dp_count, mp_count = mesh.devices.shape
    y_count = len({d.coords[1] for d in mesh.devices.flat})
    chip_cores = len({d.core_on_chip for d in mesh.devices.flat})
    grid = mesh.devices.reshape(y_count, dp_count // (y_count * chip_cores), chip_cores, mp_count)
    split = Mesh(grid, ("y", "z", "c", "mp"))
    dp = ("y", "z", "c")
    placed = (P(dp, None), P("mp", None, None), P("mp"), P("mp"), P(dp, "mp"))
    return jax.shard_map(
        body,
        mesh=split,
        in_specs=placed,
        out_specs=(P(dp, "mp"), P(dp, "mp"), P("mp", dp, None)),
        check_vma=False,
    )
```

```python
import jax
import jax.numpy as jnp
from jax import lax
from jax.sharding import Mesh, PartitionSpec as P


def gelu_tanh(inputs):
    return jax.nn.gelu(inputs, approximate=True)


def body(tokens, blocks, block_row, block_col, cotangent):
    mp_count = lax.axis_size("mp")
    token_count = tokens.shape[0]
    block_size = blocks.shape[1]
    row_blocks = tokens.shape[1] // block_size
    slot_cap = blocks.shape[0] // mp_count
    col_blocks = cotangent.shape[1] // block_size
    column_here = lax.axis_index("mp")
    w_groups = blocks.reshape(mp_count, slot_cap * block_size, block_size)
    lists = jnp.stack([block_row, block_col], 1).reshape(mp_count, 1, slot_cap * 2)
    lists = jnp.pad(lists.astype(jnp.bfloat16), ((0, 0), (0, 15), (0, block_size - slot_cap * 2)))
    sent = lax.all_to_all(jnp.concatenate([w_groups, lists], 1), "mp", 0, 0, tiled=True)
    w_here = sent[:, : slot_cap * block_size].reshape(mp_count, slot_cap, block_size, block_size)
    lists = sent[:, slot_cap * block_size, : slot_cap * 2].astype(jnp.int32).reshape(mp_count, slot_cap, 2)
    row_groups = jnp.maximum(lists[:, :, 0], 0)
    col_groups = lists[:, :, 1]
    slot_live = col_groups >= 0
    spread = tokens.reshape(token_count, row_blocks, block_size)
    picked_x = jnp.take(spread, row_groups, axis=1)
    live_mask = slot_live.astype(jnp.float32)
    parts = jnp.einsum(
        "tmck,mckn->mctn", picked_x, w_here, preferred_element_type=jnp.float32
    )
    parts = (parts * live_mask[:, :, None, None]).astype(jnp.bfloat16)
    local_col = col_groups - column_here * col_blocks
    onehot = (local_col[:, :, None] == jnp.arange(col_blocks)[None, None, :]).astype(jnp.bfloat16)
    pre_act = jnp.einsum("mctn,mcj->tjn", parts, onehot, preferred_element_type=jnp.float32)
    pre_act = pre_act.reshape(token_count, col_blocks * block_size)
    activation_f, pullback = jax.vjp(gelu_tanh, pre_act)
    activation = activation_f.astype(jnp.bfloat16)
    pre_grad = pullback(cotangent.astype(jnp.float32))[0].astype(jnp.bfloat16)
    pre_grad = pre_grad.reshape(token_count, col_blocks, block_size)
    grad_cols = jnp.einsum(
        "tjn,mcj->mctn", pre_grad, onehot, preferred_element_type=jnp.float32
    ).astype(jnp.bfloat16)
    input_terms = jnp.einsum(
        "mctn,mckn->mctk", grad_cols, w_here, preferred_element_type=jnp.float32
    )
    row_onehot = (
        (row_groups[:, :, None] == jnp.arange(row_blocks)[None, None, :]) & slot_live[:, :, None]
    ).astype(jnp.float32)
    input_partial = jnp.einsum(
        "mctk,mcr->rtk", input_terms, row_onehot, precision=lax.Precision.HIGHEST
    )
    pieces = input_partial.reshape(mp_count, row_blocks // mp_count, token_count, block_size)
    input_grad = lax.dynamic_index_in_dim(pieces, column_here, 0, keepdims=False)
    for shift in range(1, mp_count):
        piece = lax.dynamic_index_in_dim(pieces, (column_here + shift) % mp_count, 0, keepdims=False)
        ring = [(k, (k + shift) % mp_count) for k in range(mp_count)]
        input_grad = input_grad + lax.ppermute(piece, "mp", ring)
    input_grad = jnp.transpose(input_grad.astype(jnp.bfloat16), (1, 0, 2))
    input_grad = input_grad.reshape(token_count, row_blocks * block_size // mp_count)
    weight_terms = jnp.einsum(
        "tmck,mctn->mckn", picked_x, grad_cols, preferred_element_type=jnp.float32
    )
    weight_terms = weight_terms.reshape(mp_count, slot_cap * block_size, block_size)
    ny, nz, nc = lax.axis_size("y"), lax.axis_size("z"), lax.axis_size("c")
    rows = slot_cap * block_size // (ny * nz * nc)
    staged = weight_terms.reshape(mp_count, ny, nz, nc, rows, block_size)
    staged = jnp.transpose(staged, (3, 1, 2, 4, 0, 5)).reshape(nc, -1, mp_count, block_size)
    staged = lax.all_to_all(staged, "c", 0, 0, tiled=True).sum(0)
    staged = staged.reshape(ny, nz * rows, mp_count, block_size)
    staged = lax.all_to_all(staged.astype(jnp.bfloat16), "y", 0, 0, tiled=True)
    staged = staged.astype(jnp.float32).sum(0).reshape(nz, rows, mp_count, block_size)
    staged = lax.all_to_all(staged, "z", 0, 0, tiled=True).sum(0)
    staged = lax.all_to_all(staged, "mp", 1, 1, tiled=True)
    summed = jnp.transpose(staged, (1, 0, 2))
    return (activation, input_grad, summed)


def solution(mesh):
    dp_count, mp_count = mesh.devices.shape
    y_count = len({d.coords[1] for d in mesh.devices.flat})
    chip_cores = len({d.core_on_chip for d in mesh.devices.flat})
    grid = mesh.devices.reshape(y_count, dp_count // (y_count * chip_cores), chip_cores, mp_count)
    split = Mesh(grid, ("y", "z", "c", "mp"))
    dp = ("y", "z", "c")
    placed = (P(dp, None), P("mp", None, None), P("mp"), P("mp"), P(dp, "mp"))
    return jax.shard_map(
        body,
        mesh=split,
        in_specs=placed,
        out_specs=(P(dp, "mp"), P(dp, "mp"), P("mp", dp, None)),
        check_vma=False,
    )
```

```python
import jax
import jax.numpy as jnp
from jax import lax
from jax.sharding import Mesh, PartitionSpec as P


def gelu_tanh(inputs):
    return jax.nn.gelu(inputs, approximate=True)


def body(tokens, blocks, block_row, block_col, cotangent):
    mp_count = lax.axis_size("mp")
    token_count = tokens.shape[0]
    block_size = blocks.shape[1]
    row_blocks = tokens.shape[1] // block_size
    slot_cap = blocks.shape[0] // mp_count
    col_blocks = cotangent.shape[1] // block_size
    column_here = lax.axis_index("mp")
    w_groups = blocks.reshape(mp_count, slot_cap * block_size, block_size)
    lists = jnp.stack([block_row, block_col], 1).reshape(mp_count, 1, slot_cap * 2)
    lists = jnp.pad(lists.astype(jnp.bfloat16), ((0, 0), (0, 15), (0, block_size - slot_cap * 2)))
    sent = lax.all_to_all(jnp.concatenate([w_groups, lists], 1), "mp", 0, 0, tiled=True)
    w_here = sent[:, : slot_cap * block_size].reshape(mp_count, slot_cap, block_size, block_size)
    lists = sent[:, slot_cap * block_size, : slot_cap * 2].astype(jnp.int32).reshape(mp_count, slot_cap, 2)
    row_groups = jnp.maximum(lists[:, :, 0], 0)
    col_groups = lists[:, :, 1]
    slot_live = col_groups >= 0
    spread = tokens.reshape(token_count, row_blocks, block_size)
    picked_x = jnp.take(spread, row_groups, axis=1)
    live_mask = slot_live.astype(jnp.float32)
    parts = jnp.einsum(
        "tmck,mckn->mctn", picked_x, w_here, preferred_element_type=jnp.float32
    )
    parts = (parts * live_mask[:, :, None, None]).astype(jnp.bfloat16)
    local_col = col_groups - column_here * col_blocks
    onehot = (local_col[:, :, None] == jnp.arange(col_blocks)[None, None, :]).astype(jnp.bfloat16)
    pre_act = jnp.einsum("mctn,mcj->tjn", parts, onehot, preferred_element_type=jnp.float32)
    pre_act = pre_act.reshape(token_count, col_blocks * block_size)
    activation_f, pullback = jax.vjp(gelu_tanh, pre_act)
    activation = activation_f.astype(jnp.bfloat16)
    pre_grad = pullback(cotangent.astype(jnp.float32))[0].astype(jnp.bfloat16)
    pre_grad = pre_grad.reshape(token_count, col_blocks, block_size)
    grad_cols = jnp.einsum(
        "tjn,mcj->mctn", pre_grad, onehot, preferred_element_type=jnp.float32
    ).astype(jnp.bfloat16)
    input_terms = jnp.einsum(
        "mctn,mckn->mctk", grad_cols, w_here, preferred_element_type=jnp.float32
    )
    row_onehot = (
        (row_groups[:, :, None] == jnp.arange(row_blocks)[None, None, :]) & slot_live[:, :, None]
    ).astype(jnp.float32)
    input_partial = jnp.einsum(
        "mctk,mcr->rtk", input_terms, row_onehot, precision=lax.Precision.HIGHEST
    )
    pieces = input_partial.reshape(mp_count, row_blocks // mp_count, token_count, block_size)
    input_grad = lax.dynamic_index_in_dim(pieces, column_here, 0, keepdims=False)
    for shift in range(1, mp_count):
        piece = lax.dynamic_index_in_dim(pieces, (column_here + shift) % mp_count, 0, keepdims=False)
        ring = [(k, (k + shift) % mp_count) for k in range(mp_count)]
        input_grad = input_grad + lax.ppermute(piece, "mp", ring)
    input_grad = jnp.transpose(input_grad.astype(jnp.bfloat16), (1, 0, 2))
    input_grad = input_grad.reshape(token_count, row_blocks * block_size // mp_count)
    weight_terms = jnp.einsum(
        "tmck,mctn->mckn", picked_x, grad_cols, preferred_element_type=jnp.float32
    )
    weight_terms = weight_terms.reshape(mp_count, slot_cap * block_size, block_size)
    ny, nz, nc = lax.axis_size("y"), lax.axis_size("z"), lax.axis_size("c")
    rows = slot_cap * block_size // (ny * nz * nc)
    staged = weight_terms.reshape(mp_count, ny, nz, nc, rows, block_size)
    staged = jnp.transpose(staged, (3, 1, 2, 4, 0, 5)).reshape(nc, -1, mp_count, block_size)
    core_here = lax.axis_index("c")
    mine = lax.dynamic_index_in_dim(staged, core_here, 0, keepdims=False)
    other = lax.dynamic_index_in_dim(staged, 1 - core_here, 0, keepdims=False)
    staged = mine + lax.ppermute(other, "c", [(0, 1), (1, 0)])
    staged = staged.reshape(ny * nz, rows, mp_count, block_size)
    staged = lax.all_to_all(staged.astype(jnp.bfloat16), ("y", "z"), 0, 0, tiled=True)
    staged = staged.astype(jnp.float32).sum(0)
    staged = lax.all_to_all(staged, "mp", 1, 1, tiled=True)
    summed = jnp.transpose(staged, (1, 0, 2))
    return (activation, input_grad, summed)


def solution(mesh):
    dp_count, mp_count = mesh.devices.shape
    y_count = len({d.coords[1] for d in mesh.devices.flat})
    chip_cores = len({d.core_on_chip for d in mesh.devices.flat})
    grid = mesh.devices.reshape(y_count, dp_count // (y_count * chip_cores), chip_cores, mp_count)
    split = Mesh(grid, ("y", "z", "c", "mp"))
    dp = ("y", "z", "c")
    placed = (P(dp, None), P("mp", None, None), P("mp"), P("mp"), P(dp, "mp"))
    return jax.shard_map(
        body,
        mesh=split,
        in_specs=placed,
        out_specs=(P(dp, "mp"), P(dp, "mp"), P("mp", dp, None)),
        check_vma=False,
    )
```

```python
import jax
import jax.numpy as jnp
from jax import lax
from jax.sharding import Mesh, PartitionSpec as P


def gelu_tanh(inputs):
    return jax.nn.gelu(inputs, approximate=True)


def body(tokens, blocks, block_row, block_col, cotangent):
    mp_count = lax.axis_size("mp")
    token_count = tokens.shape[0]
    block_size = blocks.shape[1]
    row_blocks = tokens.shape[1] // block_size
    slot_cap = blocks.shape[0] // mp_count
    col_blocks = cotangent.shape[1] // block_size
    column_here = lax.axis_index("mp")
    w_groups = blocks.reshape(mp_count, slot_cap * block_size, block_size)
    lists = jnp.stack([block_row, block_col], 1).reshape(mp_count, 1, slot_cap * 2)
    lists = jnp.pad(lists.astype(jnp.bfloat16), ((0, 0), (0, 15), (0, block_size - slot_cap * 2)))
    sent = lax.all_to_all(jnp.concatenate([w_groups, lists], 1), "mp", 0, 0, tiled=True)
    w_here = sent[:, : slot_cap * block_size].reshape(mp_count, slot_cap, block_size, block_size)
    lists = sent[:, slot_cap * block_size, : slot_cap * 2].astype(jnp.int32).reshape(mp_count, slot_cap, 2)
    row_groups = jnp.maximum(lists[:, :, 0], 0)
    col_groups = lists[:, :, 1]
    slot_live = col_groups >= 0
    spread = tokens.reshape(token_count, row_blocks, block_size)
    picked_x = jnp.take(spread, row_groups, axis=1)
    live_mask = slot_live.astype(jnp.float32)
    parts = jnp.einsum(
        "tmck,mckn->mctn", picked_x, w_here, preferred_element_type=jnp.float32
    )
    parts = (parts * live_mask[:, :, None, None]).astype(jnp.bfloat16)
    local_col = col_groups - column_here * col_blocks
    onehot = (local_col[:, :, None] == jnp.arange(col_blocks)[None, None, :]).astype(jnp.bfloat16)
    pre_act = jnp.einsum("mctn,mcj->tjn", parts, onehot, preferred_element_type=jnp.float32)
    pre_act = pre_act.reshape(token_count, col_blocks * block_size)
    activation_f, pullback = jax.vjp(gelu_tanh, pre_act)
    activation = activation_f.astype(jnp.bfloat16)
    pre_grad = pullback(cotangent.astype(jnp.float32))[0].astype(jnp.bfloat16)
    pre_grad = pre_grad.reshape(token_count, col_blocks, block_size)
    grad_cols = jnp.einsum(
        "tjn,mcj->mctn", pre_grad, onehot, preferred_element_type=jnp.float32
    ).astype(jnp.bfloat16)
    input_terms = jnp.einsum(
        "mctn,mckn->mctk", grad_cols, w_here, preferred_element_type=jnp.float32
    )
    local_row = (row_groups - column_here * (row_blocks // mp_count)) % row_blocks
    row_onehot = (
        (local_row[:, :, None] == jnp.arange(row_blocks)[None, None, :]) & slot_live[:, :, None]
    ).astype(jnp.float32)
    input_partial = jnp.einsum(
        "mctk,mcr->rtk", input_terms, row_onehot, precision=lax.Precision.HIGHEST
    )
    pieces = input_partial.reshape(mp_count, row_blocks // mp_count, token_count, block_size)
    input_grad = pieces[0]
    for shift in range(1, mp_count):
        ring = [(k, (k + shift) % mp_count) for k in range(mp_count)]
        input_grad = input_grad + lax.ppermute(pieces[shift], "mp", ring)
    input_grad = jnp.transpose(input_grad.astype(jnp.bfloat16), (1, 0, 2))
    input_grad = input_grad.reshape(token_count, row_blocks * block_size // mp_count)
    weight_terms = jnp.einsum(
        "tmck,mctn->mckn", picked_x, grad_cols, preferred_element_type=jnp.float32
    )
    weight_terms = weight_terms.reshape(mp_count, slot_cap * block_size, block_size)
    ny, nz, nc = lax.axis_size("y"), lax.axis_size("z"), lax.axis_size("c")
    rows = slot_cap * block_size // (ny * nz * nc)
    staged = weight_terms.reshape(mp_count, ny, nz, nc, rows, block_size)
    staged = jnp.transpose(staged, (3, 1, 2, 4, 0, 5)).reshape(nc, -1, mp_count, block_size)
    staged = lax.all_to_all(staged, "c", 0, 0, tiled=True).sum(0)
    staged = staged.reshape(ny * nz, rows, mp_count, block_size)
    staged = lax.all_to_all(staged.astype(jnp.bfloat16), ("y", "z"), 0, 0, tiled=True)
    staged = staged.astype(jnp.float32).sum(0)
    staged = lax.all_to_all(staged, "mp", 1, 1, tiled=True)
    summed = jnp.transpose(staged, (1, 0, 2))
    return (activation, input_grad, summed)


def solution(mesh):
    dp_count, mp_count = mesh.devices.shape
    y_count = len({d.coords[1] for d in mesh.devices.flat})
    chip_cores = len({d.core_on_chip for d in mesh.devices.flat})
    grid = mesh.devices.reshape(y_count, dp_count // (y_count * chip_cores), chip_cores, mp_count)
    split = Mesh(grid, ("y", "z", "c", "mp"))
    dp = ("y", "z", "c")
    placed = (P(dp, None), P("mp", None, None), P("mp"), P("mp"), P(dp, "mp"))
    return jax.shard_map(
        body,
        mesh=split,
        in_specs=placed,
        out_specs=(P(dp, "mp"), P(dp, "mp"), P("mp", dp, None)),
        check_vma=False,
    )
```
